128 devices in a mesh: section: 16 (over x, z_hi, core), expert: 8 (over z_lo, y).
Axes of the slice: x: 4, y: 4, z: 4 (z_hi: 2, z_lo: 2; z = z_hi * 2 + z_lo), core: 2. Of those that a mesh axis runs over, the one named last changes fastest.
Arguments:
- grad_in: bfloat16 [16, 1024, 4096], P('section', 'expert'), may hold values from -6 to 6
- saved_inputs: bfloat16 [3, 16, 1024, 4096], P(None, 'section', 'expert'), may hold values from -6 to 6
- expert_ids: int32 [3, 16, 1024, 2], P(None, 'section', 'expert'), may hold values from 0 to 7, as said below
- slots: int32 [3, 16, 1024, 2], P(None, 'section', 'expert'), may hold values from 0 to 36, as said below
- gates: float32 [3, 16, 1024, 2], P(None, 'section', 'expert'), may hold values from 0.05 to 0.8
- w_gate: bfloat16 [16, 8, 4096, 768], P('section', 'expert'), may hold values from -0.09375 to 0.09375
- w_up: bfloat16 [16, 8, 4096, 768], P('section', 'expert'), may hold values from -0.09375 to 0.09375
- w_down: bfloat16 [16, 8, 768, 4096], P('section', 'expert'), may hold values from -0.21875 to 0.21875
Outputs:
- grad_out: bfloat16 [16, 1024, 4096], P('section', 'expert')
The draws below stay inside these ranges and needn't reach their ends.
Inputs may be any that keep to these rules, and one draw needn't show every extreme that they name: `expert_ids`: each token names 2 different experts; every expert is named. `slots`: among the routes of the tokens of one device (aligned blocks of 128 tokens) to one expert, taken in some order, the n-th has slot min(n, 36) for n = 0, 1, ...; in every round and section some such group has more than 36 routes.
All inputs are finite; a program needn't handle non-finite values.
Results may differ from the reference program's by a relative error of at most 0.0075.
Values may be sent and summed in bfloat16 or wider, within the bound.
No kernel may reach another device: no remote copies, remote signals or barrier semaphores. Data moves between devices by JAX's collectives and lax.ppermute only.
A program may use at most 128 MiB of HBM per device.

```python
import math
import jax
import jax.numpy as jnp
from jax import lax

D = 4096
HID = 768
TOPK = 2
ROUNDS = 3
T_DEV = 128
LAYER_EXPERTS = 8
TOKENS = 1024
CAP = 36
N_SECTION = 16


def route_table(key):
    base = jax.random.fold_in(key, 7)
    score_key, order_key = jax.random.split(base)
    forced_key = jax.random.fold_in(base, 11)
    router_scores = jax.random.randint(score_key, (ROUNDS, N_SECTION, TOKENS, LAYER_EXPERTS), 0, 1 << 20) * LAYER_EXPERTS + jnp.arange(LAYER_EXPERTS, dtype=jnp.int32)
    forced = jax.random.randint(forced_key, (ROUNDS, N_SECTION), 0, LAYER_EXPERTS).astype(jnp.int32)
    leading_block = jnp.arange(TOKENS, dtype=jnp.int32) // T_DEV == 0
    selected_experts = jnp.arange(LAYER_EXPERTS, dtype=jnp.int32)[None, None, None, :] == forced[:, :, None, None]
    extra_score = jnp.where(leading_block[None, None, :, None] & selected_experts, (1 << 21) * LAYER_EXPERTS, 0).astype(jnp.int32)
    router_scores = router_scores + extra_score
    route_ids = lax.top_k(router_scores, TOPK)[1].astype(jnp.int32)
    blocks = TOKENS // T_DEV
    routes = T_DEV * TOPK
    ranks = jax.random.randint(order_key, (ROUNDS, N_SECTION, blocks, routes), 0, 1 << 20) * routes + jnp.arange(routes, dtype=jnp.int32)
    flat_ids = route_ids.reshape(ROUNDS, N_SECTION, blocks, routes)
    same = flat_ids[..., :, None] == flat_ids[..., None, :]
    before = ranks[..., None, :] < ranks[..., :, None]
    slot_ids = jnp.sum((same & before).astype(jnp.int32), axis=-1).astype(jnp.int32)
    slot_ids = jnp.minimum(slot_ids, CAP).astype(jnp.int32)
    return (route_ids, slot_ids.reshape(ROUNDS, N_SECTION, TOKENS, TOPK))


def draw_expert_ids(key, part):
    return route_table(key)[0]


def draw_slots(key, part):
    return route_table(key)[1]


def block_scale(own_key, extent, shards, least, top_value):
    level = 1.0
    for axis_at, shards_of in shards:
        heights = jax.random.uniform(jax.random.fold_in(jax.random.fold_in(own_key, 6), axis_at), (shards_of,), jnp.float32, least / len(shards), top_value / len(shards))
        level = level * jnp.repeat(jnp.exp(heights), extent[axis_at] // shards_of).reshape((-1,) + (1,) * (len(extent) - 1 - axis_at))
    return level


def scatter_about(key, shape, scale, most, cuts=(), kind=jnp.bfloat16):
    factor_of = block_scale(key, shape, cuts, -0.22, 0.18) if cuts else 1.0
    entries = jax.random.normal(key, shape, jnp.float32) * scale * factor_of
    return jnp.minimum(jnp.maximum(entries, -most), most).astype(kind)


def setup_inputs(seed: int = 0) -> dict:
    streams_of = jax.random.split(jax.random.key(seed), 9)
    return {
        "grad_in": scatter_about(streams_of[0], (N_SECTION, TOKENS, D), 1.0, 6.0, ((0, 16), (1, 8))),
        "saved_inputs": scatter_about(streams_of[1], (ROUNDS, N_SECTION, TOKENS, D), 1.0, 6.0, ((1, 16), (2, 8))),
        "expert_ids": draw_expert_ids(jax.random.fold_in(streams_of[8], 71), 0),
        "slots": draw_slots(jax.random.fold_in(streams_of[8], 71), 0),
        "gates": jnp.clip(jnp.exp(math.log(0.8) - 2.7725887 * jax.random.uniform(streams_of[4], (ROUNDS, N_SECTION, TOKENS, TOPK), jnp.float32) ** block_scale(streams_of[4], (ROUNDS, N_SECTION, TOKENS, TOPK), ((1, 16), (2, 8)), -0.2, 0.2)), 0.05, 0.8),
        "w_gate": scatter_about(streams_of[5], (N_SECTION, LAYER_EXPERTS, D, HID), D ** -0.5, 0.09375, ((0, 16), (1, 8))),
        "w_up": scatter_about(streams_of[6], (N_SECTION, LAYER_EXPERTS, D, HID), D ** -0.5, 0.09375, ((0, 16), (1, 8))),
        "w_down": scatter_about(streams_of[7], (N_SECTION, LAYER_EXPERTS, HID, D), HID ** -0.5, 0.21875, ((0, 16), (1, 8))),
    }


def expert_pass(grad_part, input_part, gate_proj, up_proj, down_proj):
    pre_gate = jnp.dot(input_part, gate_proj, preferred_element_type=jnp.float32)
    pre_up = jnp.dot(input_part, up_proj, preferred_element_type=jnp.float32)
    grad_hidden = jnp.dot(grad_part, down_proj.T, preferred_element_type=jnp.float32)
    sigma = jax.nn.sigmoid(pre_gate)
    derivative = sigma * (1.0 + pre_gate * (1.0 - sigma))
    grad_gate = (grad_hidden * pre_up * derivative).astype(jnp.bfloat16)
    grad_up = (grad_hidden * pre_gate * sigma).astype(jnp.bfloat16)
    summed = jnp.dot(grad_gate, gate_proj.T, preferred_element_type=jnp.float32)
    summed = summed + jnp.dot(grad_up, up_proj.T, preferred_element_type=jnp.float32)
    return summed.astype(jnp.bfloat16)


def section_step(packed):
    grads, inputs, route_ids, slot_ids, weights, gate_stacked, up_all, down_all = packed
    token_ids = jnp.arange(TOKENS, dtype=jnp.int32)
    source = token_ids // T_DEV
    row_total = LAYER_EXPERTS * LAYER_EXPERTS * CAP
    positions = jnp.where(slot_ids < CAP, (source[:, None] * LAYER_EXPERTS + route_ids) * CAP + slot_ids, row_total).astype(jnp.int32)
    owners = jnp.broadcast_to(token_ids[:, None], positions.shape).reshape(-1)
    sources = jnp.full((row_total,), TOKENS, jnp.int32).at[positions.reshape(-1)].set(owners, mode="drop")
    grad_buffer = jnp.take(grads, sources, axis=0, mode="fill", fill_value=0).reshape(LAYER_EXPERTS, LAYER_EXPERTS, CAP, D)
    input_buffer = jnp.take(inputs, sources, axis=0, mode="fill", fill_value=0).reshape(LAYER_EXPERTS, LAYER_EXPERTS, CAP, D)

    def per_expert(expert):
        grad_part = grad_buffer[:, expert].reshape(LAYER_EXPERTS * CAP, D)
        input_part = input_buffer[:, expert].reshape(LAYER_EXPERTS * CAP, D)
        result = expert_pass(grad_part, input_part, gate_stacked[expert], up_all[expert], down_all[expert])
        return result.reshape(LAYER_EXPERTS, CAP, D)

    arrived = lax.map(per_expert, jnp.arange(LAYER_EXPERTS, dtype=jnp.int32))
    arrived = jnp.transpose(arrived, (1, 0, 2, 3)).reshape(row_total, D)
    picked = jnp.take(arrived, positions, axis=0, mode="fill", fill_value=0)
    summed = grads.astype(jnp.float32) + jnp.sum(weights[..., None] * picked.astype(jnp.float32), axis=1)
    return summed.astype(jnp.bfloat16)


def reference(grad_in, saved_inputs, expert_ids, slots, gates, w_gate, w_up, w_down):
    present_block = grad_in
    for step in range(ROUNDS):
        layer_grad = lax.map(section_step, (present_block, saved_inputs[step], expert_ids[step], slots[step], gates[step], w_gate, w_up, w_down))
        present_block = jnp.roll(layer_grad, -1, axis=0)
    return present_block
```

```python
import jax
import jax.numpy as jnp
from jax import lax
from jax.sharding import PartitionSpec as P


def shifted(x, axis, by):
    devices = lax.axis_size(axis)
    return lax.ppermute(x, axis, [(i, (i + by) % devices) for i in range(devices)])


def forward_part(input_part, gate_proj, up_proj):
    pre_gate = jnp.dot(input_part, gate_proj, preferred_element_type=jnp.float32)
    pre_up = jnp.dot(input_part, up_proj, preferred_element_type=jnp.float32)
    return pre_gate, pre_up


def backward_part(grad_part, pre_gate, pre_up, gate_proj, up_proj, down_proj):
    grad_hidden = jnp.dot(grad_part, down_proj.T, preferred_element_type=jnp.float32)
    sigma = jax.nn.sigmoid(pre_gate)
    derivative = sigma * (1.0 + pre_gate * (1.0 - sigma))
    grad_gate = (grad_hidden * pre_up * derivative).astype(jnp.bfloat16)
    grad_up = (grad_hidden * pre_gate * sigma).astype(jnp.bfloat16)
    summed = jnp.dot(grad_gate, gate_proj.T, preferred_element_type=jnp.float32)
    summed = summed + jnp.dot(grad_up, up_proj.T, preferred_element_type=jnp.float32)
    return summed.astype(jnp.bfloat16)


def per_device(grad_in, saved_inputs, expert_ids, slots, gates, w_gate, w_up, w_down):
    groups = lax.axis_size("expert")
    rows_dev = grad_in.shape[1]
    width = grad_in.shape[2]
    rounds = saved_inputs.shape[0]
    capacity = 9 * rows_dev * expert_ids.shape[-1] // (8 * groups)
    padded = -(-capacity // 16) * 16
    columns = groups * padded
    gate_proj = w_gate[0, 0]
    up_proj = w_up[0, 0]
    down_proj = w_down[0, 0]
    column_ids = jnp.arange(columns, dtype=jnp.int32)

    def route_plan(step):
        route_ids = expert_ids[step, 0]
        slot_ids = slots[step, 0]
        target = jnp.where(slot_ids < capacity, route_ids * padded + slot_ids, -1)
        hit = target[:, :, None] == column_ids[None, None, :]
        dispatch = jnp.any(hit, axis=1).T.astype(jnp.bfloat16)
        weights = jnp.sum(jnp.where(hit, gates[step, 0][:, :, None], 0.0), axis=1)
        weights_hi = weights.astype(jnp.bfloat16)
        weights_lo = (weights - weights_hi.astype(jnp.float32)).astype(jnp.bfloat16)
        return dispatch, weights_hi, weights_lo

    def collect(dispatch, rows):
        picked = jnp.dot(dispatch, rows, preferred_element_type=jnp.float32)
        return picked.astype(jnp.bfloat16).reshape(groups, padded, width)

    def exchange(buffer):
        moved = lax.all_to_all(buffer, "expert", split_axis=0, concat_axis=0, tiled=True)
        return moved.reshape(columns, width)

    plans = [route_plan(step) for step in range(rounds)]
    forwards = []
    for step in range(rounds):
        input_part = exchange(collect(plans[step][0], saved_inputs[step, 0]))
        forwards.append(forward_part(input_part, gate_proj, up_proj))

    present_block = grad_in[0]
    for step in range(rounds):
        dispatch, weights_hi, weights_lo = plans[step]
        grad_part = exchange(collect(dispatch, present_block))
        pre_gate, pre_up = forwards[step]
        result = backward_part(grad_part, pre_gate, pre_up, gate_proj, up_proj, down_proj)
        arrived = exchange(result.reshape(groups, padded, width))
        combined = jnp.dot(weights_hi, arrived, preferred_element_type=jnp.float32)
        combined = combined + jnp.dot(weights_lo, arrived, preferred_element_type=jnp.float32)
        summed = present_block.astype(jnp.float32) + combined
        present_block = shifted(summed.astype(jnp.bfloat16), "section", -1)
    return present_block[None]


def solution(mesh):
    placed = (
        P("section", "expert", None),
        P(None, "section", "expert", None),
        P(None, "section", "expert", None),
        P(None, "section", "expert", None),
        P(None, "section", "expert", None),
        P("section", "expert", None, None),
        P("section", "expert", None, None),
        P("section", "expert", None, None),
    )
    return jax.shard_map(
        per_device,
        mesh=mesh,
        in_specs=placed,
        out_specs=P("section", "expert", None),
        check_vma=False,
    )
```

```python
import jax
import jax.numpy as jnp
from jax import lax
from jax.sharding import PartitionSpec as P


def shifted(x, axis, by):
    devices = lax.axis_size(axis)
    return lax.ppermute(x, axis, [(i, (i + by) % devices) for i in range(devices)])


def forward_part(input_part, gate_proj, up_proj):
    pre_gate = jnp.einsum("scjl,jlh->sch", input_part, gate_proj, preferred_element_type=jnp.float32)
    pre_up = jnp.einsum("scjl,jlh->sch", input_part, up_proj, preferred_element_type=jnp.float32)
    return pre_gate, pre_up


def backward_part(grad_part, pre_gate, pre_up, gate_proj, up_proj, down_proj):
    grad_hidden = jnp.einsum("scjl,hjl->sch", grad_part, down_proj, preferred_element_type=jnp.float32)
    sigma = jax.nn.sigmoid(pre_gate)
    derivative = sigma * (1.0 + pre_gate * (1.0 - sigma))
    grad_gate = (grad_hidden * pre_up * derivative).astype(jnp.bfloat16)
    grad_up = (grad_hidden * pre_gate * sigma).astype(jnp.bfloat16)
    summed = jnp.einsum("sch,jlh->scjl", grad_gate, gate_proj, preferred_element_type=jnp.float32)
    summed = summed + jnp.einsum("sch,jlh->scjl", grad_up, up_proj, preferred_element_type=jnp.float32)
    return summed.astype(jnp.bfloat16)


def per_device(grad_in, saved_inputs, expert_ids, slots, gates, w_gate, w_up, w_down):
    groups = lax.axis_size("expert")
    rows_dev = grad_in.shape[1]
    width = grad_in.shape[2]
    rounds = saved_inputs.shape[0]
    capacity = 9 * rows_dev * expert_ids.shape[-1] // (8 * groups)
    lanes = 128
    pieces = width // lanes
    columns = groups * capacity
    hidden = w_gate.shape[-1]
    gate_proj = w_gate[0, 0].reshape(pieces, lanes, hidden)
    up_proj = w_up[0, 0].reshape(pieces, lanes, hidden)
    down_proj = w_down[0, 0].reshape(hidden, pieces, lanes)
    column_ids = jnp.arange(columns, dtype=jnp.int32)

    def route_plan(step):
        route_ids = expert_ids[step, 0]
        slot_ids = slots[step, 0]
        target = jnp.where(slot_ids < capacity, route_ids * capacity + slot_ids, -1)
        hit = target[:, :, None] == column_ids[None, None, :]
        dispatch = jnp.any(hit, axis=1).T.astype(jnp.bfloat16).reshape(groups, capacity, rows_dev)
        weights = jnp.sum(jnp.where(hit, gates[step, 0][:, :, None], 0.0), axis=1)
        weights_hi = weights.astype(jnp.bfloat16)
        weights_lo = (weights - weights_hi.astype(jnp.float32)).astype(jnp.bfloat16)
        shape = (rows_dev, groups, capacity)
        return dispatch, weights_hi.reshape(shape), weights_lo.reshape(shape)

    def collect(dispatch, rows):
        picked = jnp.einsum("ect,tjl->ecjl", dispatch, rows, preferred_element_type=jnp.float32)
        return picked.astype(jnp.bfloat16)

    def exchange(buffer):
        flat = buffer.reshape(groups, capacity * pieces, lanes)
        moved = lax.all_to_all(flat, "expert", split_axis=0, concat_axis=0, tiled=True)
        return moved.reshape(groups, capacity, pieces, lanes)

    plans = [route_plan(step) for step in range(rounds)]
    forwards = []
    for step in range(rounds):
        rows = saved_inputs[step, 0].reshape(rows_dev, pieces, lanes)
        input_part = exchange(collect(plans[step][0], rows))
        forwards.append(forward_part(input_part, gate_proj, up_proj))

    present_block = grad_in[0].reshape(rows_dev, pieces, lanes)
    for step in range(rounds):
        dispatch, weights_hi, weights_lo = plans[step]
        grad_part = exchange(collect(dispatch, present_block))
        pre_gate, pre_up = forwards[step]
        result = backward_part(grad_part, pre_gate, pre_up, gate_proj, up_proj, down_proj)
        arrived = exchange(result)
        combined = jnp.einsum("tec,ecjl->tjl", weights_hi, arrived, preferred_element_type=jnp.float32)
        combined = combined + jnp.einsum("tec,ecjl->tjl", weights_lo, arrived, preferred_element_type=jnp.float32)
        summed = present_block.astype(jnp.float32) + combined
        present_block = shifted(summed.astype(jnp.bfloat16), "section", -1)
    return present_block.reshape(1, rows_dev, width)


def solution(mesh):
    placed = (
        P("section", "expert", None),
        P(None, "section", "expert", None),
        P(None, "section", "expert", None),
        P(None, "section", "expert", None),
        P(None, "section", "expert", None),
        P("section", "expert", None, None),
        P("section", "expert", None, None),
        P("section", "expert", None, None),
    )
    return jax.shard_map(
        per_device,
        mesh=mesh,
        in_specs=placed,
        out_specs=P("section", "expert", None),
        check_vma=False,
    )
```

```python
import jax
import jax.numpy as jnp
from jax import lax
from jax.sharding import PartitionSpec as P


def shifted(x, axis, by):
    devices = lax.axis_size(axis)
    return lax.ppermute(x, axis, [(i, (i + by) % devices) for i in range(devices)])


def forward_part(input_part, gate_proj, up_proj):
    pre_gate = jnp.einsum("scjl,jlh->sch", input_part, gate_proj, preferred_element_type=jnp.float32)
    pre_up = jnp.einsum("scjl,jlh->sch", input_part, up_proj, preferred_element_type=jnp.float32)
    return pre_gate, pre_up


def backward_part(grad_part, pre_gate, pre_up, gate_proj, up_proj, down_proj):
    grad_hidden = jnp.einsum("scjl,hjl->sch", grad_part, down_proj, preferred_element_type=jnp.float32)
    sigma = jax.nn.sigmoid(pre_gate)
    derivative = sigma * (1.0 + pre_gate * (1.0 - sigma))
    grad_gate = (grad_hidden * pre_up * derivative).astype(jnp.bfloat16)
    grad_up = (grad_hidden * pre_gate * sigma).astype(jnp.bfloat16)
    summed = jnp.einsum("sch,jlh->scjl", grad_gate, gate_proj, preferred_element_type=jnp.float32)
    summed = summed + jnp.einsum("sch,jlh->scjl", grad_up, up_proj, preferred_element_type=jnp.float32)
    return summed.astype(jnp.bfloat16)


def per_device(grad_in, saved_inputs, expert_ids, slots, gates, w_gate, w_up, w_down):
    groups = lax.axis_size("expert")
    rows_dev = grad_in.shape[1]
    width = grad_in.shape[2]
    rounds = saved_inputs.shape[0]
    capacity = 9 * rows_dev * expert_ids.shape[-1] // (8 * groups)
    lanes = 128
    pieces = width // lanes
    columns = groups * capacity
    hidden = w_gate.shape[-1]
    gate_proj = w_gate[0, 0].reshape(pieces, lanes, hidden)
    up_proj = w_up[0, 0].reshape(pieces, lanes, hidden)
    down_proj = w_down[0, 0].reshape(hidden, pieces, lanes)
    column_ids = jnp.arange(columns, dtype=jnp.int32)

    def route_plan(step):
        route_ids = expert_ids[step, 0]
        slot_ids = slots[step, 0]
        target = jnp.where(slot_ids < capacity, route_ids * capacity + slot_ids, -1)
        hit = target[:, :, None] == column_ids[None, None, :]
        dispatch = jnp.any(hit, axis=1).T.astype(jnp.bfloat16).reshape(groups, capacity, rows_dev)
        weights = jnp.sum(jnp.where(hit, gates[step, 0][:, :, None], 0.0), axis=1)
        weights_hi = weights.astype(jnp.bfloat16)
        weights_lo = (weights - weights_hi.astype(jnp.float32)).astype(jnp.bfloat16)
        shape = (rows_dev, groups, capacity)
        return dispatch, weights_hi.reshape(shape), weights_lo.reshape(shape)

    def collect(dispatch, rows):
        picked = jnp.einsum("ect,tjl->ecjl", dispatch, rows, preferred_element_type=jnp.float32)
        return picked.astype(jnp.bfloat16)

    def exchange(buffer):
        flat = buffer.reshape(groups, capacity * pieces, lanes)
        moved = lax.all_to_all(flat, "expert", split_axis=0, concat_axis=0, tiled=True)
        return moved.reshape(groups, capacity, pieces, lanes)

    plans = [route_plan(step) for step in range(rounds)]
    input_buffers = [
        collect(plans[step][0], saved_inputs[step, 0].reshape(rows_dev, pieces, lanes))
        for step in range(rounds)
    ]
    pre_gate, pre_up = forward_part(exchange(input_buffers[0]), gate_proj, up_proj)

    present_block = grad_in[0].reshape(rows_dev, pieces, lanes)
    for step in range(rounds):
        dispatch, weights_hi, weights_lo = plans[step]
        grad_part = exchange(collect(dispatch, present_block))
        if step + 1 < rounds:
            grad_part, next_buffer = lax.optimization_barrier((grad_part, input_buffers[step + 1]))
            next_part = exchange(next_buffer)
        result = backward_part(grad_part, pre_gate, pre_up, gate_proj, up_proj, down_proj)
        if step + 1 < rounds:
            result, next_part = lax.optimization_barrier((result, next_part))
            pre_gate, pre_up = forward_part(next_part, gate_proj, up_proj)
        arrived = exchange(result)
        combined = jnp.einsum("tec,ecjl->tjl", weights_hi, arrived, preferred_element_type=jnp.float32)
        combined = combined + jnp.einsum("tec,ecjl->tjl", weights_lo, arrived, preferred_element_type=jnp.float32)
        summed = present_block.astype(jnp.float32) + combined
        present_block = shifted(summed.astype(jnp.bfloat16), "section", -1)
    return present_block.reshape(1, rows_dev, width)


def solution(mesh):
    placed = (
        P("section", "expert", None),
        P(None, "section", "expert", None),
        P(None, "section", "expert", None),
        P(None, "section", "expert", None),
        P(None, "section", "expert", None),
        P("section", "expert", None, None),
        P("section", "expert", None, None),
        P("section", "expert", None, None),
    )
    return jax.shard_map(
        per_device,
        mesh=mesh,
        in_specs=placed,
        out_specs=P("section", "expert", None),
        check_vma=False,
    )
```

```python
import jax
import jax.numpy as jnp
from jax import lax
from jax.sharding import PartitionSpec as P


def shifted(x, axis, by):
    devices = lax.axis_size(axis)
    return lax.ppermute(x, axis, [(i, (i + by) % devices) for i in range(devices)])


def forward_part(input_part, gate_proj, up_proj):
    pre_gate = jnp.einsum("scjl,jlh->sch", input_part, gate_proj, preferred_element_type=jnp.float32)
    pre_up = jnp.einsum("scjl,jlh->sch", input_part, up_proj, preferred_element_type=jnp.float32)
    return pre_gate, pre_up


def backward_part(grad_part, pre_gate, pre_up, gate_proj, up_proj, down_proj):
    grad_hidden = jnp.einsum("scjl,hjl->sch", grad_part, down_proj, preferred_element_type=jnp.float32)
    sigma = jax.nn.sigmoid(pre_gate)
    derivative = sigma * (1.0 + pre_gate * (1.0 - sigma))
    grad_gate = (grad_hidden * pre_up * derivative).astype(jnp.bfloat16)
    grad_up = (grad_hidden * pre_gate * sigma).astype(jnp.bfloat16)
    summed = jnp.einsum("sch,jlh->scjl", grad_gate, gate_proj, preferred_element_type=jnp.float32)
    summed = summed + jnp.einsum("sch,jlh->scjl", grad_up, up_proj, preferred_element_type=jnp.float32)
    return summed.astype(jnp.bfloat16)


def per_device(grad_in, saved_inputs, expert_ids, slots, gates, w_gate, w_up, w_down):
    groups = lax.axis_size("expert")
    rows_dev = grad_in.shape[1]
    width = grad_in.shape[2]
    rounds = saved_inputs.shape[0]
    capacity = 9 * rows_dev * expert_ids.shape[-1] // (8 * groups)
    lanes = 128
    pieces = width // lanes
    columns = groups * capacity
    hidden = w_gate.shape[-1]
    gate_proj = w_gate[0, 0].reshape(pieces, lanes, hidden)
    up_proj = w_up[0, 0].reshape(pieces, lanes, hidden)
    down_proj = w_down[0, 0].reshape(hidden, pieces, lanes)
    column_ids = jnp.arange(columns, dtype=jnp.int32)

    def route_plan(step):
        route_ids = expert_ids[step, 0]
        slot_ids = slots[step, 0]
        target = jnp.where(slot_ids < capacity, route_ids * capacity + slot_ids, -1)
        hit = target[:, :, None] == column_ids[None, None, :]
        dispatch = jnp.any(hit, axis=1).T.astype(jnp.bfloat16).reshape(groups, capacity, rows_dev)
        weights = jnp.sum(jnp.where(hit, gates[step, 0][:, :, None], 0.0), axis=1)
        weights_hi = weights.astype(jnp.bfloat16)
        weights_lo = (weights - weights_hi.astype(jnp.float32)).astype(jnp.bfloat16)
        shape = (rows_dev, groups, capacity)
        return dispatch, weights_hi.reshape(shape), weights_lo.reshape(shape)

    def collect(dispatch, rows):
        picked = jnp.einsum("ect,tjl->ecjl", dispatch, rows, preferred_element_type=jnp.float32)
        return picked.astype(jnp.bfloat16)

    def exchange(buffer):
        count = buffer.shape[1]
        flat = buffer.reshape(groups, count * pieces, lanes)
        moved = lax.all_to_all(flat, "expert", split_axis=0, concat_axis=0, tiled=True)
        return moved.reshape(groups, count, pieces, lanes)

    plans = [route_plan(step) for step in range(rounds)]
    input_buffers = [
        collect(plans[step][0], saved_inputs[step, 0].reshape(rows_dev, pieces, lanes))
        for step in range(rounds)
    ]
    first_part = exchange(input_buffers[0])
    first_part, first_block = lax.optimization_barrier((first_part, grad_in[0]))
    pre_gate, pre_up = forward_part(first_part, gate_proj, up_proj)
    bounds = [(0, capacity // 2), (capacity // 2, capacity)]

    present_block = first_block.reshape(rows_dev, pieces, lanes)
    for step in range(rounds):
        dispatch, weights_hi, weights_lo = plans[step]
        grad_parts = [exchange(collect(dispatch[:, lo:hi], present_block)) for lo, hi in bounds]
        if step + 1 < rounds:
            grad_parts[1], next_buffer = lax.optimization_barrier((grad_parts[1], input_buffers[step + 1]))
            next_part = exchange(next_buffer)
        results = [
            backward_part(grad_parts[i], pre_gate[:, lo:hi], pre_up[:, lo:hi], gate_proj, up_proj, down_proj)
            for i, (lo, hi) in enumerate(bounds)
        ]
        if step + 1 < rounds:
            results[0], next_part = lax.optimization_barrier((results[0], next_part))
            pre_gate, pre_up = forward_part(next_part, gate_proj, up_proj)
        summed = present_block.astype(jnp.float32)
        for i, (lo, hi) in enumerate(bounds):
            arrived = exchange(results[i])
            summed = summed + jnp.einsum(
                "tec,ecjl->tjl", weights_hi[:, :, lo:hi], arrived, preferred_element_type=jnp.float32
            )
            summed = summed + jnp.einsum(
                "tec,ecjl->tjl", weights_lo[:, :, lo:hi], arrived, preferred_element_type=jnp.float32
            )
        present_block = shifted(summed.astype(jnp.bfloat16), "section", -1)
    return present_block.reshape(1, rows_dev, width)


def solution(mesh):
    placed = (
        P("section", "expert", None),
        P(None, "section", "expert", None),
        P(None, "section", "expert", None),
        P(None, "section", "expert", None),
        P(None, "section", "expert", None),
        P("section", "expert", None, None),
        P("section", "expert", None, None),
        P("section", "expert", None, None),
    )
    return jax.shard_map(
        per_device,
        mesh=mesh,
        in_specs=placed,
        out_specs=P("section", "expert", None),
        check_vma=False,
    )
```

```python
import jax
import jax.numpy as jnp
from jax import lax
from jax.sharding import PartitionSpec as P


def shifted(x, axis, by):
    devices = lax.axis_size(axis)
    return lax.ppermute(x, axis, [(i, (i + by) % devices) for i in range(devices)])


def forward_part(input_part, joint_proj):
    return jnp.einsum("scjl,jlh->sch", input_part, joint_proj, preferred_element_type=jnp.float32)


def backward_part(grad_part, pre_joint, joint_proj, down_proj):
    hidden = down_proj.shape[0]
    pre_gate = pre_joint[..., :hidden]
    pre_up = pre_joint[..., hidden:]
    grad_hidden = jnp.einsum("scjl,hjl->sch", grad_part, down_proj, preferred_element_type=jnp.float32)
    sigma = jax.nn.sigmoid(pre_gate)
    derivative = sigma * (1.0 + pre_gate * (1.0 - sigma))
    grad_gate = (grad_hidden * pre_up * derivative).astype(jnp.bfloat16)
    grad_up = (grad_hidden * pre_gate * sigma).astype(jnp.bfloat16)
    grad_joint = jnp.concatenate([grad_gate, grad_up], axis=-1)
    summed = jnp.einsum("sch,jlh->scjl", grad_joint, joint_proj, preferred_element_type=jnp.float32)
    return summed.astype(jnp.bfloat16)


def per_device(grad_in, saved_inputs, expert_ids, slots, gates, w_gate, w_up, w_down):
    groups = lax.axis_size("expert")
    rows_dev = grad_in.shape[1]
    width = grad_in.shape[2]
    rounds = saved_inputs.shape[0]
    capacity = 9 * rows_dev * expert_ids.shape[-1] // (8 * groups)
    lanes = 128
    pieces = width // lanes
    columns = groups * capacity
    hidden = w_gate.shape[-1]
    joint_proj = jnp.concatenate([w_gate[0, 0], w_up[0, 0]], axis=1).reshape(pieces, lanes, 2 * hidden)
    down_proj = w_down[0, 0].reshape(hidden, pieces, lanes)
    column_ids = jnp.arange(columns, dtype=jnp.int32)

    def route_plan(step):
        route_ids = expert_ids[step, 0]
        slot_ids = slots[step, 0]
        target = jnp.where(slot_ids < capacity, route_ids * capacity + slot_ids, -1)
        hit = target[:, :, None] == column_ids[None, None, :]
        dispatch = jnp.any(hit, axis=1).T.astype(jnp.bfloat16).reshape(groups, capacity, rows_dev)
        weights = jnp.sum(jnp.where(hit, gates[step, 0][:, :, None], 0.0), axis=1)
        weights_hi = weights.astype(jnp.bfloat16)
        weights_lo = (weights - weights_hi.astype(jnp.float32)).astype(jnp.bfloat16)
        shape = (rows_dev, groups, capacity)
        return dispatch, weights_hi.reshape(shape), weights_lo.reshape(shape)

    def collect(dispatch, rows):
        picked = jnp.einsum("ect,tjl->ecjl", dispatch, rows, preferred_element_type=jnp.float32)
        return picked.astype(jnp.bfloat16)

    def exchange(buffer):
        count = buffer.shape[1]
        flat = buffer.reshape(groups, count * pieces, lanes)
        moved = lax.all_to_all(flat, "expert", split_axis=0, concat_axis=0, tiled=True)
        return moved.reshape(groups, count, pieces, lanes)

    plans = [route_plan(step) for step in range(rounds)]
    input_buffers = [
        collect(plans[step][0], saved_inputs[step, 0].reshape(rows_dev, pieces, lanes))
        for step in range(rounds)
    ]
    first_part = exchange(input_buffers[0])
    first_part, first_block = lax.optimization_barrier((first_part, grad_in[0]))
    pre_joint = forward_part(first_part, joint_proj)
    bounds = [(0, capacity // 2), (capacity // 2, capacity)]

    present_block = first_block.reshape(rows_dev, pieces, lanes)
    for step in range(rounds):
        dispatch, weights_hi, weights_lo = plans[step]
        grad_parts = [exchange(collect(dispatch[:, lo:hi], present_block)) for lo, hi in bounds]
        if step + 1 < rounds:
            grad_parts[1], next_buffer = lax.optimization_barrier((grad_parts[1], input_buffers[step + 1]))
            next_part = exchange(next_buffer)
        results = [
            backward_part(grad_parts[i], pre_joint[:, lo:hi], joint_proj, down_proj)
            for i, (lo, hi) in enumerate(bounds)
        ]
        if step + 1 < rounds:
            results[0], next_part = lax.optimization_barrier((results[0], next_part))
            pre_joint = forward_part(next_part, joint_proj)
        summed = present_block.astype(jnp.float32)
        for i, (lo, hi) in enumerate(bounds):
            arrived = exchange(results[i])
            summed = summed + jnp.einsum(
                "tec,ecjl->tjl", weights_hi[:, :, lo:hi], arrived, preferred_element_type=jnp.float32
            )
            summed = summed + jnp.einsum(
                "tec,ecjl->tjl", weights_lo[:, :, lo:hi], arrived, preferred_element_type=jnp.float32
            )
        present_block = shifted(summed.astype(jnp.bfloat16), "section", -1)
    return present_block.reshape(1, rows_dev, width)


def solution(mesh):
    placed = (
        P("section", "expert", None),
        P(None, "section", "expert", None),
        P(None, "section", "expert", None),
        P(None, "section", "expert", None),
        P(None, "section", "expert", None),
        P("section", "expert", None, None),
        P("section", "expert", None, None),
        P("section", "expert", None, None),
    )
    return jax.shard_map(
        per_device,
        mesh=mesh,
        in_specs=placed,
        out_specs=P("section", "expert", None),
        check_vma=False,
    )
```

```python
import jax
import jax.numpy as jnp
from jax import lax
from jax.sharding import PartitionSpec as P


def shifted(x, axis, by):
    devices = lax.axis_size(axis)
    return lax.ppermute(x, axis, [(i, (i + by) % devices) for i in range(devices)])


def forward_part(input_part, gate_proj, up_proj):
    pre_gate = jnp.einsum("scjl,jlh->sch", input_part, gate_proj, preferred_element_type=jnp.float32)
    pre_up = jnp.einsum("scjl,jlh->sch", input_part, up_proj, preferred_element_type=jnp.float32)
    return pre_gate, pre_up


def backward_part(grad_part, pre_gate, pre_up, gate_proj, up_proj, down_proj):
    grad_hidden = jnp.einsum("scjl,hjl->sch", grad_part, down_proj, preferred_element_type=jnp.float32)
    sigma = jax.nn.sigmoid(pre_gate)
    derivative = sigma * (1.0 + pre_gate * (1.0 - sigma))
    grad_gate = (grad_hidden * pre_up * derivative).astype(jnp.bfloat16)
    grad_up = (grad_hidden * pre_gate * sigma).astype(jnp.bfloat16)
    summed = jnp.einsum("sch,jlh->scjl", grad_gate, gate_proj, preferred_element_type=jnp.float32)
    summed = summed + jnp.einsum("sch,jlh->scjl", grad_up, up_proj, preferred_element_type=jnp.float32)
    return summed.astype(jnp.bfloat16)


def per_device(grad_in, saved_inputs, expert_ids, slots, gates, w_gate, w_up, w_down):
    groups = lax.axis_size("expert")
    rows_dev = grad_in.shape[1]
    width = grad_in.shape[2]
    rounds = saved_inputs.shape[0]
    capacity = 9 * rows_dev * expert_ids.shape[-1] // (8 * groups)
    lanes = 128
    pieces = width // lanes
    columns = groups * capacity
    hidden = w_gate.shape[-1]
    gate_proj = w_gate[0, 0].reshape(pieces, lanes, hidden)
    up_proj = w_up[0, 0].reshape(pieces, lanes, hidden)
    down_proj = w_down[0, 0].reshape(hidden, pieces, lanes)
    column_ids = jnp.arange(columns, dtype=jnp.int32)

    def route_plan(step):
        route_ids = expert_ids[step, 0]
        slot_ids = slots[step, 0]
        target = jnp.where(slot_ids < capacity, route_ids * capacity + slot_ids, -1)
        hit = target[:, :, None] == column_ids[None, None, :]
        dispatch = jnp.any(hit, axis=1).T.astype(jnp.bfloat16).reshape(groups, capacity, rows_dev)
        weights = jnp.sum(jnp.where(hit, gates[step, 0][:, :, None], 0.0), axis=1)
        weights_hi = weights.astype(jnp.bfloat16)
        weights_lo = (weights - weights_hi.astype(jnp.float32)).astype(jnp.bfloat16)
        shape = (rows_dev, groups, capacity)
        return dispatch, weights_hi.reshape(shape), weights_lo.reshape(shape)

    def collect(dispatch, rows):
        picked = jnp.einsum("ect,tjl->ecjl", dispatch, rows, preferred_element_type=jnp.float32)
        return picked.astype(jnp.bfloat16)

    def exchange(buffer):
        count = buffer.shape[1]
        flat = buffer.reshape(groups, count * pieces, lanes)
        moved = lax.all_to_all(flat, "expert", split_axis=0, concat_axis=0, tiled=True)
        return moved.reshape(groups, count, pieces, lanes)

    plans = [route_plan(step) for step in range(rounds)]
    input_buffers = [
        collect(plans[step][0], saved_inputs[step, 0].reshape(rows_dev, pieces, lanes))
        for step in range(rounds)
    ]
    present_block = grad_in[0].reshape(rows_dev, pieces, lanes)
    first = exchange(jnp.concatenate([input_buffers[0], collect(plans[0][0], present_block)], axis=1))
    pre_gate, pre_up = forward_part(first[:, :capacity], gate_proj, up_proj)
    bounds = [(0, capacity // 2), (capacity // 2, capacity)]

    for step in range(rounds):
        dispatch, weights_hi, weights_lo = plans[step]
        if step == 0:
            grad_part = first[:, capacity:]
        else:
            grad_part = exchange(collect(dispatch, present_block))
        if step + 1 < rounds:
            grad_part, next_buffer = lax.optimization_barrier((grad_part, input_buffers[step + 1]))
            next_part = exchange(next_buffer)
        grad_parts = [grad_part[:, lo:hi] for lo, hi in bounds]
        results = [
            backward_part(grad_parts[i], pre_gate[:, lo:hi], pre_up[:, lo:hi], gate_proj, up_proj, down_proj)
            for i, (lo, hi) in enumerate(bounds)
        ]
        if step + 1 < rounds:
            results[0], next_part = lax.optimization_barrier((results[0], next_part))
            pre_gate, pre_up = forward_part(next_part, gate_proj, up_proj)
        summed = present_block.astype(jnp.float32)
        for i, (lo, hi) in enumerate(bounds):
            arrived = exchange(results[i])
            summed = summed + jnp.einsum(
                "tec,ecjl->tjl", weights_hi[:, :, lo:hi], arrived, preferred_element_type=jnp.float32
            )
            summed = summed + jnp.einsum(
                "tec,ecjl->tjl", weights_lo[:, :, lo:hi], arrived, preferred_element_type=jnp.float32
            )
        present_block = shifted(summed.astype(jnp.bfloat16), "section", -1)
    return present_block.reshape(1, rows_dev, width)


def solution(mesh):
    placed = (
        P("section", "expert", None),
        P(None, "section", "expert", None),
        P(None, "section", "expert", None),
        P(None, "section", "expert", None),
        P(None, "section", "expert", None),
        P("section", "expert", None, None),
        P("section", "expert", None, None),
        P("section", "expert", None, None),
    )
    return jax.shard_map(
        per_device,
        mesh=mesh,
        in_specs=placed,
        out_specs=P("section", "expert", None),
        check_vma=False,
    )
```

```python
import jax
import jax.numpy as jnp
from jax import lax
from jax.sharding import PartitionSpec as P


def shifted(x, axis, by):
    devices = lax.axis_size(axis)
    return lax.ppermute(x, axis, [(i, (i + by) % devices) for i in range(devices)])


def forward_part(input_part, gate_proj, up_proj):
    pre_gate = jnp.einsum("scjl,jlh->sch", input_part, gate_proj, preferred_element_type=jnp.float32)
    pre_up = jnp.einsum("scjl,jlh->sch", input_part, up_proj, preferred_element_type=jnp.float32)
    return pre_gate, pre_up


def backward_part(grad_part, pre_gate, pre_up, gate_proj, up_proj, down_proj):
    grad_hidden = jnp.einsum("scjl,hjl->sch", grad_part, down_proj, preferred_element_type=jnp.float32)
    sigma = jax.nn.sigmoid(pre_gate)
    derivative = sigma * (1.0 + pre_gate * (1.0 - sigma))
    grad_gate = (grad_hidden * pre_up * derivative).astype(jnp.bfloat16)
    grad_up = (grad_hidden * pre_gate * sigma).astype(jnp.bfloat16)
    summed = jnp.einsum("sch,jlh->scjl", grad_gate, gate_proj, preferred_element_type=jnp.float32)
    summed = summed + jnp.einsum("sch,jlh->scjl", grad_up, up_proj, preferred_element_type=jnp.float32)
    return summed.astype(jnp.bfloat16)


def per_device(grad_in, saved_inputs, expert_ids, slots, gates, w_gate, w_up, w_down):
    groups = lax.axis_size("expert")
    rows_dev = grad_in.shape[1]
    width = grad_in.shape[2]
    rounds = saved_inputs.shape[0]
    capacity = 9 * rows_dev * expert_ids.shape[-1] // (8 * groups)
    lanes = 128
    pieces = width // lanes
    columns = groups * capacity
    hidden = w_gate.shape[-1]
    gate_proj = w_gate[0, 0].reshape(pieces, lanes, hidden)
    up_proj = w_up[0, 0].reshape(pieces, lanes, hidden)
    down_proj = w_down[0, 0].reshape(hidden, pieces, lanes)
    column_ids = jnp.arange(columns, dtype=jnp.int32)

    def route_plan(step):
        route_ids = expert_ids[step, 0]
        slot_ids = slots[step, 0]
        target = jnp.where(slot_ids < capacity, route_ids * capacity + slot_ids, -1)
        hit = target[:, :, None] == column_ids[None, None, :]
        dispatch = jnp.any(hit, axis=1).T.astype(jnp.bfloat16).reshape(groups, capacity, rows_dev)
        weights = jnp.sum(jnp.where(hit, gates[step, 0][:, :, None], 0.0), axis=1)
        weights_hi = weights.astype(jnp.bfloat16)
        weights_lo = (weights - weights_hi.astype(jnp.float32)).astype(jnp.bfloat16)
        shape = (rows_dev, groups, capacity)
        return dispatch, weights_hi.reshape(shape), weights_lo.reshape(shape)

    def collect(dispatch, rows):
        picked = jnp.einsum("ect,tjl->ecjl", dispatch, rows, preferred_element_type=jnp.float32)
        return picked.astype(jnp.bfloat16)

    def exchange(buffer):
        count = buffer.shape[1]
        flat = buffer.reshape(groups, count * pieces, lanes)
        moved = lax.all_to_all(flat, "expert", split_axis=0, concat_axis=0, tiled=True)
        return moved.reshape(groups, count, pieces, lanes)

    plans = [route_plan(step) for step in range(rounds)]
    input_buffers = [
        collect(plans[step][0], saved_inputs[step, 0].reshape(rows_dev, pieces, lanes))
        for step in range(rounds)
    ]
    first_part = exchange(input_buffers[0])
    first_part, first_block = lax.optimization_barrier((first_part, grad_in[0]))
    pre_gate, pre_up = forward_part(first_part, gate_proj, up_proj)
    bounds = [(0, capacity // 2), (capacity // 2, capacity)]

    present_block = first_block.reshape(rows_dev, pieces, lanes)
    for step in range(rounds):
        dispatch, weights_hi, weights_lo = plans[step]
        if step > 0:
            next_part, present_block = lax.optimization_barrier((next_part, present_block))
        grad_parts = [exchange(collect(dispatch[:, lo:hi], present_block)) for lo, hi in bounds]
        if step > 0:
            pre_gate, pre_up = forward_part(next_part, gate_proj, up_proj)
        results = [
            backward_part(grad_parts[i], pre_gate[:, lo:hi], pre_up[:, lo:hi], gate_proj, up_proj, down_proj)
            for i, (lo, hi) in enumerate(bounds)
        ]
        summed = present_block.astype(jnp.float32)
        for i, (lo, hi) in enumerate(bounds):
            arrived = exchange(results[i])
            if i + 1 == len(bounds) and step + 1 < rounds:
                arrived, next_buffer = lax.optimization_barrier((arrived, input_buffers[step + 1]))
                next_part = exchange(next_buffer)
            summed = summed + jnp.einsum(
                "tec,ecjl->tjl", weights_hi[:, :, lo:hi], arrived, preferred_element_type=jnp.float32
            )
            summed = summed + jnp.einsum(
                "tec,ecjl->tjl", weights_lo[:, :, lo:hi], arrived, preferred_element_type=jnp.float32
            )
        present_block = shifted(summed.astype(jnp.bfloat16), "section", -1)
    return present_block.reshape(1, rows_dev, width)


def solution(mesh):
    placed = (
        P("section", "expert", None),
        P(None, "section", "expert", None),
        P(None, "section", "expert", None),
        P(None, "section", "expert", None),
        P(None, "section", "expert", None),
        P("section", "expert", None, None),
        P("section", "expert", None, None),
        P("section", "expert", None, None),
    )
    return jax.shard_map(
        per_device,
        mesh=mesh,
        in_specs=placed,
        out_specs=P("section", "expert", None),
        check_vma=False,
    )
```

```python
import jax
import jax.numpy as jnp
from jax import lax
from jax.sharding import PartitionSpec as P


def shifted(x, axis, by):
    devices = lax.axis_size(axis)
    return lax.ppermute(x, axis, [(i, (i + by) % devices) for i in range(devices)])


def forward_part(input_part, gate_proj, up_proj):
    pre_gate = jnp.einsum("scjl,jlh->sch", input_part, gate_proj, preferred_element_type=jnp.float32)
    pre_up = jnp.einsum("scjl,jlh->sch", input_part, up_proj, preferred_element_type=jnp.float32)
    return pre_gate, pre_up


def backward_part(grad_part, pre_gate, pre_up, gate_proj, up_proj, down_proj):
    grad_hidden = jnp.einsum("scjl,hjl->sch", grad_part, down_proj, preferred_element_type=jnp.float32)
    sigma = jax.nn.sigmoid(pre_gate)
    derivative = sigma * (1.0 + pre_gate * (1.0 - sigma))
    grad_gate = (grad_hidden * pre_up * derivative).astype(jnp.bfloat16)
    grad_up = (grad_hidden * pre_gate * sigma).astype(jnp.bfloat16)
    summed = jnp.einsum("sch,jlh->scjl", grad_gate, gate_proj, preferred_element_type=jnp.float32)
    summed = summed + jnp.einsum("sch,jlh->scjl", grad_up, up_proj, preferred_element_type=jnp.float32)
    return summed.astype(jnp.bfloat16)


def per_device(grad_in, saved_inputs, expert_ids, slots, gates, w_gate, w_up, w_down):
    groups = lax.axis_size("expert")
    rows_dev = grad_in.shape[1]
    width = grad_in.shape[2]
    rounds = saved_inputs.shape[0]
    capacity = 9 * rows_dev * expert_ids.shape[-1] // (8 * groups)
    lanes = 128
    pieces = width // lanes
    columns = groups * capacity
    hidden = w_gate.shape[-1]
    gate_proj = w_gate[0, 0].reshape(pieces, lanes, hidden)
    up_proj = w_up[0, 0].reshape(pieces, lanes, hidden)
    down_proj = w_down[0, 0].reshape(hidden, pieces, lanes)
    column_ids = jnp.arange(columns, dtype=jnp.int32)

    def route_plan(step):
        route_ids = expert_ids[step, 0]
        slot_ids = slots[step, 0]
        target = jnp.where(slot_ids < capacity, route_ids * capacity + slot_ids, -1)
        hit = target[:, :, None] == column_ids[None, None, :]
        dispatch = jnp.any(hit, axis=1).T.astype(jnp.bfloat16).reshape(groups, capacity, rows_dev)
        weights = jnp.sum(jnp.where(hit, gates[step, 0][:, :, None], 0.0), axis=1)
        weights_hi = weights.astype(jnp.bfloat16)
        weights_lo = (weights - weights_hi.astype(jnp.float32)).astype(jnp.bfloat16)
        shape = (rows_dev, groups, capacity)
        return dispatch, weights_hi.reshape(shape), weights_lo.reshape(shape)

    def collect(dispatch, rows):
        picked = jnp.einsum("ect,tjl->ecjl", dispatch, rows, preferred_element_type=jnp.float32)
        return picked.astype(jnp.bfloat16)

    def exchange(buffer):
        count = buffer.shape[1]
        flat = buffer.reshape(groups, count * pieces, lanes)
        moved = lax.all_to_all(flat, "expert", split_axis=0, concat_axis=0, tiled=True)
        return moved.reshape(groups, count, pieces, lanes)

    plans = [route_plan(step) for step in range(rounds)]
    input_buffers = [
        collect(plans[step][0], saved_inputs[step, 0].reshape(rows_dev, pieces, lanes))
        for step in range(rounds)
    ]
    bounds = [(0, capacity // 2), (capacity // 2, capacity)]
    present_block = grad_in[0].reshape(rows_dev, pieces, lanes)
    first = exchange(
        jnp.concatenate([input_buffers[0], collect(plans[0][0][:, : bounds[0][1]], present_block)], axis=1)
    )
    pre_gate, pre_up = forward_part(first[:, :capacity], gate_proj, up_proj)

    for step in range(rounds):
        dispatch, weights_hi, weights_lo = plans[step]
        grad_parts = [
            first[:, capacity:] if step == 0 and i == 0 else exchange(collect(dispatch[:, lo:hi], present_block))
            for i, (lo, hi) in enumerate(bounds)
        ]
        if step > 0:
            pre_gate, pre_up = forward_part(next_part, gate_proj, up_proj)
        results = [
            backward_part(grad_parts[i], pre_gate[:, lo:hi], pre_up[:, lo:hi], gate_proj, up_proj, down_proj)
            for i, (lo, hi) in enumerate(bounds)
        ]
        summed = present_block.astype(jnp.float32)
        for i, (lo, hi) in enumerate(bounds):
            if i + 1 == len(bounds) and step + 1 < rounds:
                both = exchange(jnp.concatenate([results[i], input_buffers[step + 1]], axis=1))
                arrived = both[:, : hi - lo]
                next_part = both[:, hi - lo :]
            else:
                arrived = exchange(results[i])
            summed = summed + jnp.einsum(
                "tec,ecjl->tjl", weights_hi[:, :, lo:hi], arrived, preferred_element_type=jnp.float32
            )
            summed = summed + jnp.einsum(
                "tec,ecjl->tjl", weights_lo[:, :, lo:hi], arrived, preferred_element_type=jnp.float32
            )
        present_block = shifted(summed.astype(jnp.bfloat16), "section", -1)
    return present_block.reshape(1, rows_dev, width)


def solution(mesh):
    placed = (
        P("section", "expert", None),
        P(None, "section", "expert", None),
        P(None, "section", "expert", None),
        P(None, "section", "expert", None),
        P(None, "section", "expert", None),
        P("section", "expert", None, None),
        P("section", "expert", None, None),
        P("section", "expert", None, None),
    )
    return jax.shard_map(
        per_device,
        mesh=mesh,
        in_specs=placed,
        out_specs=P("section", "expert", None),
        check_vma=False,
    )
```

```python
import jax
import jax.numpy as jnp
from jax import lax
from jax.sharding import PartitionSpec as P


def shifted(x, axis, by):
    devices = lax.axis_size(axis)
    return lax.ppermute(x, axis, [(i, (i + by) % devices) for i in range(devices)])


def forward_part(input_part, gate_proj, up_proj):
    pre_gate = jnp.einsum("scjl,jlh->sch", input_part, gate_proj, preferred_element_type=jnp.float32)
    pre_up = jnp.einsum("scjl,jlh->sch", input_part, up_proj, preferred_element_type=jnp.float32)
    return pre_gate, pre_up


def backward_part(grad_part, pre_gate, pre_up, gate_proj, up_proj, down_proj):
    grad_hidden = jnp.einsum("scjl,hjl->sch", grad_part, down_proj, preferred_element_type=jnp.float32)
    sigma = jax.nn.sigmoid(pre_gate)
    derivative = sigma * (1.0 + pre_gate * (1.0 - sigma))
    grad_gate = (grad_hidden * pre_up * derivative).astype(jnp.bfloat16)
    grad_up = (grad_hidden * pre_gate * sigma).astype(jnp.bfloat16)
    summed = jnp.einsum("sch,jlh->scjl", grad_gate, gate_proj, preferred_element_type=jnp.float32)
    summed = summed + jnp.einsum("sch,jlh->scjl", grad_up, up_proj, preferred_element_type=jnp.float32)
    return summed.astype(jnp.bfloat16)


def per_device(grad_in, saved_inputs, expert_ids, slots, gates, w_gate, w_up, w_down):
    groups = lax.axis_size("expert")
    rows_dev = grad_in.shape[1]
    width = grad_in.shape[2]
    rounds = saved_inputs.shape[0]
    capacity = 9 * rows_dev * expert_ids.shape[-1] // (8 * groups)
    lanes = 128
    pieces = width // lanes
    columns = groups * capacity
    hidden = w_gate.shape[-1]
    gate_proj = w_gate[0, 0].reshape(pieces, lanes, hidden)
    up_proj = w_up[0, 0].reshape(pieces, lanes, hidden)
    down_proj = w_down[0, 0].reshape(hidden, pieces, lanes)
    column_ids = jnp.arange(columns, dtype=jnp.int32)

    def route_plan(step):
        route_ids = expert_ids[step, 0]
        slot_ids = slots[step, 0]
        target = jnp.where(slot_ids < capacity, route_ids * capacity + slot_ids, -1)
        hit = target[:, :, None] == column_ids[None, None, :]
        dispatch = jnp.any(hit, axis=1).T.astype(jnp.bfloat16).reshape(groups, capacity, rows_dev)
        weights = jnp.sum(jnp.where(hit, gates[step, 0][:, :, None], 0.0), axis=1)
        weights_hi = weights.astype(jnp.bfloat16)
        weights_lo = (weights - weights_hi.astype(jnp.float32)).astype(jnp.bfloat16)
        shape = (rows_dev, groups, capacity)
        return dispatch, weights_hi.reshape(shape), weights_lo.reshape(shape)

    def collect(dispatch, rows):
        picked = jnp.einsum("ect,tjl->ecjl", dispatch, rows, preferred_element_type=jnp.float32)
        return picked.astype(jnp.bfloat16)

    def exchange(buffer):
        count = buffer.shape[1]
        flat = buffer.reshape(groups, count * pieces, lanes)
        moved = lax.all_to_all(flat, "expert", split_axis=0, concat_axis=0, tiled=True)
        return moved.reshape(groups, count, pieces, lanes)

    def send_around(buffer):
        parts = [buffer[0]] + [
            lax.ppermute(buffer[k], "expert", [(i, (i + k) % groups) for i in range(groups)])
            for k in range(1, groups)
        ]
        return jnp.stack(parts)

    position = lax.axis_index("expert")
    rotation = (position + jnp.arange(groups, dtype=jnp.int32)) % groups
    restore = (position - jnp.arange(groups, dtype=jnp.int32)) % groups

    plans = [route_plan(step) for step in range(rounds)]
    input_buffers = [
        collect(
            plans[step][0] if step == 0 else jnp.take(plans[step][0], rotation, axis=0),
            saved_inputs[step, 0].reshape(rows_dev, pieces, lanes),
        )
        for step in range(rounds)
    ]
    first_part = exchange(input_buffers[0])
    first_part, first_block = lax.optimization_barrier((first_part, grad_in[0]))
    pre_gate, pre_up = forward_part(first_part, gate_proj, up_proj)
    bounds = [(0, capacity // 2), (capacity // 2, capacity)]

    present_block = first_block.reshape(rows_dev, pieces, lanes)
    for step in range(rounds):
        dispatch, weights_hi, weights_lo = plans[step]
        grad_parts = [exchange(collect(dispatch[:, lo:hi], present_block)) for lo, hi in bounds]
        if step > 0:
            pre_gate, pre_up = forward_part(next_part, gate_proj, up_proj)
            pre_gate = jnp.take(pre_gate, restore, axis=0)
            pre_up = jnp.take(pre_up, restore, axis=0)
        if step + 1 < rounds:
            grad_parts[0], next_buffer = lax.optimization_barrier((grad_parts[0], input_buffers[step + 1]))
            next_part = send_around(next_buffer)
        results = [
            backward_part(grad_parts[i], pre_gate[:, lo:hi], pre_up[:, lo:hi], gate_proj, up_proj, down_proj)
            for i, (lo, hi) in enumerate(bounds)
        ]
        summed = present_block.astype(jnp.float32)
        for i, (lo, hi) in enumerate(bounds):
            arrived = exchange(results[i])
            summed = summed + jnp.einsum(
                "tec,ecjl->tjl", weights_hi[:, :, lo:hi], arrived, preferred_element_type=jnp.float32
            )
            summed = summed + jnp.einsum(
                "tec,ecjl->tjl", weights_lo[:, :, lo:hi], arrived, preferred_element_type=jnp.float32
            )
        present_block = shifted(summed.astype(jnp.bfloat16), "section", -1)
    return present_block.reshape(1, rows_dev, width)


def solution(mesh):
    placed = (
        P("section", "expert", None),
        P(None, "section", "expert", None),
        P(None, "section", "expert", None),
        P(None, "section", "expert", None),
        P(None, "section", "expert", None),
        P("section", "expert", None, None),
        P("section", "expert", None, None),
        P("section", "expert", None, None),
    )
    return jax.shard_map(
        per_device,
        mesh=mesh,
        in_specs=placed,
        out_specs=P("section", "expert", None),
        check_vma=False,
    )
```

```python
import jax
import jax.numpy as jnp
from jax import lax
from jax.sharding import PartitionSpec as P


def shifted(x, axis, by):
    devices = lax.axis_size(axis)
    return lax.ppermute(x, axis, [(i, (i + by) % devices) for i in range(devices)])


def forward_part(input_part, gate_proj, up_proj):
    pre_gate = jnp.einsum("scjl,jlh->sch", input_part, gate_proj, preferred_element_type=jnp.float32)
    pre_up = jnp.einsum("scjl,jlh->sch", input_part, up_proj, preferred_element_type=jnp.float32)
    return pre_gate, pre_up


def backward_part(grad_part, pre_gate, pre_up, gate_proj, up_proj, down_proj):
    grad_hidden = jnp.einsum("scjl,hjl->sch", grad_part, down_proj, preferred_element_type=jnp.float32)
    sigma = jax.nn.sigmoid(pre_gate)
    derivative = sigma * (1.0 + pre_gate * (1.0 - sigma))
    grad_gate = (grad_hidden * pre_up * derivative).astype(jnp.bfloat16)
    grad_up = (grad_hidden * pre_gate * sigma).astype(jnp.bfloat16)
    summed = jnp.einsum("sch,jlh->scjl", grad_gate, gate_proj, preferred_element_type=jnp.float32)
    summed = summed + jnp.einsum("sch,jlh->scjl", grad_up, up_proj, preferred_element_type=jnp.float32)
    return summed.astype(jnp.bfloat16)


def per_device(grad_in, saved_inputs, expert_ids, slots, gates, w_gate, w_up, w_down):
    groups = lax.axis_size("expert")
    rows_dev = grad_in.shape[1]
    width = grad_in.shape[2]
    rounds = saved_inputs.shape[0]
    capacity = 9 * rows_dev * expert_ids.shape[-1] // (8 * groups)
    lanes = 128
    pieces = width // lanes
    columns = groups * capacity
    hidden = w_gate.shape[-1]
    gate_proj = w_gate[0, 0].reshape(pieces, lanes, hidden)
    up_proj = w_up[0, 0].reshape(pieces, lanes, hidden)
    down_proj = w_down[0, 0].reshape(hidden, pieces, lanes)
    column_ids = jnp.arange(columns, dtype=jnp.int32)

    def route_plan(step):
        route_ids = expert_ids[step, 0]
        slot_ids = slots[step, 0]
        target = jnp.where(slot_ids < capacity, route_ids * capacity + slot_ids, -1)
        hit = target[:, :, None] == column_ids[None, None, :]
        dispatch = jnp.any(hit, axis=1).T.astype(jnp.bfloat16).reshape(groups, capacity, rows_dev)
        weights = jnp.sum(jnp.where(hit, gates[step, 0][:, :, None], 0.0), axis=1)
        weights_hi = weights.astype(jnp.bfloat16)
        weights_lo = (weights - weights_hi.astype(jnp.float32)).astype(jnp.bfloat16)
        shape = (rows_dev, groups, capacity)
        return dispatch, weights_hi.reshape(shape), weights_lo.reshape(shape)

    def collect(dispatch, rows):
        picked = jnp.einsum("ect,tjl->ecjl", dispatch, rows, preferred_element_type=jnp.float32)
        return picked.astype(jnp.bfloat16)

    def exchange(buffer):
        count = buffer.shape[1]
        flat = buffer.reshape(groups, count * pieces, lanes)
        moved = lax.all_to_all(flat, "expert", split_axis=0, concat_axis=0, tiled=True)
        return moved.reshape(groups, count, pieces, lanes)

    plans = [route_plan(step) for step in range(rounds)]
    first_part = exchange(collect(plans[0][0], saved_inputs[0, 0].reshape(rows_dev, pieces, lanes)))
    first_part, first_block, later_inputs = lax.optimization_barrier((first_part, grad_in[0], saved_inputs[1:]))
    input_buffers = [None] + [
        collect(plans[step][0], later_inputs[step - 1, 0].reshape(rows_dev, pieces, lanes))
        for step in range(1, rounds)
    ]
    pre_gate, pre_up = forward_part(first_part, gate_proj, up_proj)
    bounds = [(0, capacity // 2), (capacity // 2, capacity)]

    present_block = first_block.reshape(rows_dev, pieces, lanes)
    for step in range(rounds):
        dispatch, weights_hi, weights_lo = plans[step]
        if step > 0:
            next_part, present_block = lax.optimization_barrier((next_part, present_block))
        grad_parts = [exchange(collect(dispatch[:, lo:hi], present_block)) for lo, hi in bounds]
        if step > 0:
            pre_gate, pre_up = forward_part(next_part, gate_proj, up_proj)
        results = [
            backward_part(grad_parts[i], pre_gate[:, lo:hi], pre_up[:, lo:hi], gate_proj, up_proj, down_proj)
            for i, (lo, hi) in enumerate(bounds)
        ]
        summed = present_block.astype(jnp.float32)
        for i, (lo, hi) in enumerate(bounds):
            arrived = exchange(results[i])
            if i + 1 == len(bounds) and step + 1 < rounds:
                arrived, next_buffer = lax.optimization_barrier((arrived, input_buffers[step + 1]))
                next_part = exchange(next_buffer)
            summed = summed + jnp.einsum(
                "tec,ecjl->tjl", weights_hi[:, :, lo:hi], arrived, preferred_element_type=jnp.float32
            )
            summed = summed + jnp.einsum(
                "tec,ecjl->tjl", weights_lo[:, :, lo:hi], arrived, preferred_element_type=jnp.float32
            )
        present_block = shifted(summed.astype(jnp.bfloat16), "section", -1)
    return present_block.reshape(1, rows_dev, width)


def solution(mesh):
    placed = (
        P("section", "expert", None),
        P(None, "section", "expert", None),
        P(None, "section", "expert", None),
        P(None, "section", "expert", None),
        P(None, "section", "expert", None),
        P("section", "expert", None, None),
        P("section", "expert", None, None),
        P("section", "expert", None, None),
    )
    return jax.shard_map(
        per_device,
        mesh=mesh,
        in_specs=placed,
        out_specs=P("section", "expert", None),
        check_vma=False,
    )
```

```python
import jax
import jax.numpy as jnp
from jax import lax
from jax.sharding import PartitionSpec as P


def shifted(x, axis, by):
    devices = lax.axis_size(axis)
    return lax.ppermute(x, axis, [(i, (i + by) % devices) for i in range(devices)])


def forward_part(input_part, gate_proj, up_proj):
    pre_gate = jnp.einsum("scjl,jlh->sch", input_part, gate_proj, preferred_element_type=jnp.float32)
    pre_up = jnp.einsum("scjl,jlh->sch", input_part, up_proj, preferred_element_type=jnp.float32)
    return pre_gate, pre_up


def backward_part(grad_part, pre_gate, pre_up, gate_proj, up_proj, down_proj):
    grad_hidden = jnp.einsum("scjl,hjl->sch", grad_part, down_proj, preferred_element_type=jnp.float32)
    sigma = jax.nn.sigmoid(pre_gate)
    derivative = sigma * (1.0 + pre_gate * (1.0 - sigma))
    grad_gate = (grad_hidden * pre_up * derivative).astype(jnp.bfloat16)
    grad_up = (grad_hidden * pre_gate * sigma).astype(jnp.bfloat16)
    summed = jnp.einsum("sch,jlh->scjl", grad_gate, gate_proj, preferred_element_type=jnp.float32)
    summed = summed + jnp.einsum("sch,jlh->scjl", grad_up, up_proj, preferred_element_type=jnp.float32)
    return summed.astype(jnp.bfloat16)


def per_device(grad_in, saved_inputs, expert_ids, slots, gates, w_gate, w_up, w_down):
    groups = lax.axis_size("expert")
    rows_dev = grad_in.shape[1]
    width = grad_in.shape[2]
    rounds = saved_inputs.shape[0]
    capacity = 9 * rows_dev * expert_ids.shape[-1] // (8 * groups)
    lanes = 128
    pieces = width // lanes
    columns = groups * capacity
    hidden = w_gate.shape[-1]
    gate_proj = w_gate[0, 0].reshape(pieces, lanes, hidden)
    up_proj = w_up[0, 0].reshape(pieces, lanes, hidden)
    down_proj = w_down[0, 0].reshape(hidden, pieces, lanes)
    column_ids = jnp.arange(columns, dtype=jnp.int32)

    def route_plan(step):
        route_ids = expert_ids[step, 0]
        slot_ids = slots[step, 0]
        target = jnp.where(slot_ids < capacity, route_ids * capacity + slot_ids, -1)
        hit = target[:, :, None] == column_ids[None, None, :]
        dispatch = jnp.any(hit, axis=1).T.astype(jnp.bfloat16).reshape(groups, capacity, rows_dev)
        weights = jnp.sum(jnp.where(hit, gates[step, 0][:, :, None], 0.0), axis=1)
        weights_hi = weights.astype(jnp.bfloat16)
        weights_lo = (weights - weights_hi.astype(jnp.float32)).astype(jnp.bfloat16)
        shape = (rows_dev, groups, capacity)
        return dispatch, weights_hi.reshape(shape), weights_lo.reshape(shape)

    def collect(dispatch, rows):
        picked = jnp.einsum("ect,tjl->ecjl", dispatch, rows, preferred_element_type=jnp.float32)
        return picked.astype(jnp.bfloat16)

    def exchange(buffer):
        count = buffer.shape[1]
        flat = buffer.reshape(groups, count * pieces, lanes)
        moved = lax.all_to_all(flat, "expert", split_axis=0, concat_axis=0, tiled=True)
        return moved.reshape(groups, count, pieces, lanes)

    plans = [route_plan(step) for step in range(rounds)]
    first_part = exchange(collect(plans[0][0], saved_inputs[0, 0].reshape(rows_dev, pieces, lanes)))
    first_part, first_block, later_inputs = lax.optimization_barrier((first_part, grad_in[0], saved_inputs[1:]))
    input_buffers = [None] + [
        collect(plans[step][0], later_inputs[step - 1, 0].reshape(rows_dev, pieces, lanes))
        for step in range(1, rounds)
    ]
    pre_gate, pre_up = forward_part(first_part, gate_proj, up_proj)
    bounds = [(0, capacity // 2), (capacity // 2, capacity)]

    present_block = first_block.reshape(rows_dev, pieces, lanes)
    for step in range(rounds):
        dispatch, weights_hi, weights_lo = plans[step]
        grad_buffers = [collect(dispatch[:, lo:hi], present_block) for lo, hi in bounds]
        if step > 0:
            next_part, grad_buffers[0] = lax.optimization_barrier((next_part, grad_buffers[0]))
        grad_parts = [exchange(buffer) for buffer in grad_buffers]
        if step > 0:
            pre_gate, pre_up = forward_part(next_part, gate_proj, up_proj)
        results = [
            backward_part(grad_parts[i], pre_gate[:, lo:hi], pre_up[:, lo:hi], gate_proj, up_proj, down_proj)
            for i, (lo, hi) in enumerate(bounds)
        ]
        summed = present_block.astype(jnp.float32)
        for i, (lo, hi) in enumerate(bounds):
            arrived = exchange(results[i])
            if i + 1 == len(bounds) and step + 1 < rounds:
                arrived, next_buffer = lax.optimization_barrier((arrived, input_buffers[step + 1]))
                next_part = exchange(next_buffer)
            summed = summed + jnp.einsum(
                "tec,ecjl->tjl", weights_hi[:, :, lo:hi], arrived, preferred_element_type=jnp.float32
            )
            summed = summed + jnp.einsum(
                "tec,ecjl->tjl", weights_lo[:, :, lo:hi], arrived, preferred_element_type=jnp.float32
            )
        present_block = shifted(summed.astype(jnp.bfloat16), "section", -1)
    return present_block.reshape(1, rows_dev, width)


def solution(mesh):
    placed = (
        P("section", "expert", None),
        P(None, "section", "expert", None),
        P(None, "section", "expert", None),
        P(None, "section", "expert", None),
        P(None, "section", "expert", None),
        P("section", "expert", None, None),
        P("section", "expert", None, None),
        P("section", "expert", None, None),
    )
    return jax.shard_map(
        per_device,
        mesh=mesh,
        in_specs=placed,
        out_specs=P("section", "expert", None),
        check_vma=False,
    )
```

```python
import jax
import jax.numpy as jnp
from jax import lax
from jax.sharding import PartitionSpec as P


def shifted(x, axis, by):
    devices = lax.axis_size(axis)
    return lax.ppermute(x, axis, [(i, (i + by) % devices) for i in range(devices)])


def forward_part(input_part, gate_proj, up_proj):
    pre_gate = jnp.einsum("scjl,jlh->sch", input_part, gate_proj, preferred_element_type=jnp.float32)
    pre_up = jnp.einsum("scjl,jlh->sch", input_part, up_proj, preferred_element_type=jnp.float32)
    return pre_gate, pre_up


def backward_part(grad_part, pre_gate, pre_up, gate_proj, up_proj, down_proj):
    grad_hidden = jnp.einsum("scjl,hjl->sch", grad_part, down_proj, preferred_element_type=jnp.float32)
    sigma = jax.nn.sigmoid(pre_gate)
    derivative = sigma * (1.0 + pre_gate * (1.0 - sigma))
    grad_gate = (grad_hidden * pre_up * derivative).astype(jnp.bfloat16)
    grad_up = (grad_hidden * pre_gate * sigma).astype(jnp.bfloat16)
    summed = jnp.einsum("sch,jlh->scjl", grad_gate, gate_proj, preferred_element_type=jnp.float32)
    summed = summed + jnp.einsum("sch,jlh->scjl", grad_up, up_proj, preferred_element_type=jnp.float32)
    return summed.astype(jnp.bfloat16)


def per_device(grad_in, saved_inputs, expert_ids, slots, gates, w_gate, w_up, w_down):
    groups = lax.axis_size("expert")
    rows_dev = grad_in.shape[1]
    width = grad_in.shape[2]
    rounds = saved_inputs.shape[0]
    capacity = 9 * rows_dev * expert_ids.shape[-1] // (8 * groups)
    lanes = 128
    pieces = width // lanes
    columns = groups * capacity
    hidden = w_gate.shape[-1]
    gate_proj = w_gate[0, 0].reshape(pieces, lanes, hidden)
    up_proj = w_up[0, 0].reshape(pieces, lanes, hidden)
    down_proj = w_down[0, 0].reshape(hidden, pieces, lanes)
    column_ids = jnp.arange(columns, dtype=jnp.int32)

    def route_plan(step):
        route_ids = expert_ids[step, 0]
        slot_ids = slots[step, 0]
        target = jnp.where(slot_ids < capacity, route_ids * capacity + slot_ids, -1)
        hit = target[:, :, None] == column_ids[None, None, :]
        dispatch = jnp.any(hit, axis=1).T.astype(jnp.bfloat16).reshape(groups, capacity, rows_dev)
        weights = jnp.sum(jnp.where(hit, gates[step, 0][:, :, None], 0.0), axis=1)
        weights_hi = weights.astype(jnp.bfloat16)
        weights_lo = (weights - weights_hi.astype(jnp.float32)).astype(jnp.bfloat16)
        shape = (rows_dev, groups, capacity)
        return dispatch, weights_hi.reshape(shape), weights_lo.reshape(shape)

    def collect(dispatch, rows):
        picked = jnp.einsum("ect,tjl->ecjl", dispatch, rows, preferred_element_type=jnp.float32)
        return picked.astype(jnp.bfloat16)

    def exchange(buffer):
        count = buffer.shape[1]
        flat = buffer.reshape(groups, count * pieces, lanes)
        moved = lax.all_to_all(flat, "expert", split_axis=0, concat_axis=0, tiled=True)
        return moved.reshape(groups, count, pieces, lanes)

    plans = [route_plan(step) for step in range(rounds)]
    first_part = exchange(collect(plans[0][0], saved_inputs[0, 0].reshape(rows_dev, pieces, lanes)))
    first_part, first_block, later_inputs = lax.optimization_barrier((first_part, grad_in[0], saved_inputs[1:]))
    input_buffers = [None] + [
        collect(plans[step][0], later_inputs[step - 1, 0].reshape(rows_dev, pieces, lanes))
        for step in range(1, rounds)
    ]
    forwards = [forward_part(first_part, gate_proj, up_proj)]
    if rounds > 1:
        second_part = exchange(input_buffers[1])
        second_part, first_block = lax.optimization_barrier((second_part, first_block))
        forwards.append(forward_part(second_part, gate_proj, up_proj))
    bounds = [(0, capacity // 2), (capacity // 2, capacity)]

    present_block = first_block.reshape(rows_dev, pieces, lanes)
    for step in range(rounds):
        dispatch, weights_hi, weights_lo = plans[step]
        if step == 1 and rounds > 2:
            next_part, present_block = lax.optimization_barrier((next_part, present_block))
            forwards.append(forward_part(next_part, gate_proj, up_proj))
        grad_parts = [exchange(collect(dispatch[:, lo:hi], present_block)) for lo, hi in bounds]
        pre_gate, pre_up = forwards[step]
        results = [
            backward_part(grad_parts[i], pre_gate[:, lo:hi], pre_up[:, lo:hi], gate_proj, up_proj, down_proj)
            for i, (lo, hi) in enumerate(bounds)
        ]
        summed = present_block.astype(jnp.float32)
        for i, (lo, hi) in enumerate(bounds):
            arrived = exchange(results[i])
            if i + 1 == len(bounds) and step == 0 and rounds > 2:
                arrived, next_buffer = lax.optimization_barrier((arrived, input_buffers[2]))
                next_part = exchange(next_buffer)
            summed = summed + jnp.einsum(
                "tec,ecjl->tjl", weights_hi[:, :, lo:hi], arrived, preferred_element_type=jnp.float32
            )
            summed = summed + jnp.einsum(
                "tec,ecjl->tjl", weights_lo[:, :, lo:hi], arrived, preferred_element_type=jnp.float32
            )
        present_block = shifted(summed.astype(jnp.bfloat16), "section", -1)
    return present_block.reshape(1, rows_dev, width)


def solution(mesh):
    placed = (
        P("section", "expert", None),
        P(None, "section", "expert", None),
        P(None, "section", "expert", None),
        P(None, "section", "expert", None),
        P(None, "section", "expert", None),
        P("section", "expert", None, None),
        P("section", "expert", None, None),
        P("section", "expert", None, None),
    )
    return jax.shard_map(
        per_device,
        mesh=mesh,
        in_specs=placed,
        out_specs=P("section", "expert", None),
        check_vma=False,
    )
```

```python
import jax
import jax.numpy as jnp
from jax import lax
from jax.sharding import PartitionSpec as P


def shifted(x, axis, by):
    devices = lax.axis_size(axis)
    return lax.ppermute(x, axis, [(i, (i + by) % devices) for i in range(devices)])


def forward_part(input_part, gate_proj, up_proj):
    pre_gate = jnp.einsum("scjl,jlh->sch", input_part, gate_proj, preferred_element_type=jnp.float32)
    pre_up = jnp.einsum("scjl,jlh->sch", input_part, up_proj, preferred_element_type=jnp.float32)
    return pre_gate, pre_up


def backward_part(grad_part, pre_gate, pre_up, gate_proj, up_proj, down_proj):
    grad_hidden = jnp.einsum("scjl,hjl->sch", grad_part, down_proj, preferred_element_type=jnp.float32)
    sigma = jax.nn.sigmoid(pre_gate)
    derivative = sigma * (1.0 + pre_gate * (1.0 - sigma))
    grad_gate = (grad_hidden * pre_up * derivative).astype(jnp.bfloat16)
    grad_up = (grad_hidden * pre_gate * sigma).astype(jnp.bfloat16)
    summed = jnp.einsum("sch,jlh->scjl", grad_gate, gate_proj, preferred_element_type=jnp.float32)
    summed = summed + jnp.einsum("sch,jlh->scjl", grad_up, up_proj, preferred_element_type=jnp.float32)
    return summed.astype(jnp.bfloat16)


def per_device(grad_in, saved_inputs, expert_ids, slots, gates, w_gate, w_up, w_down):
    groups = lax.axis_size("expert")
    rows_dev = grad_in.shape[1]
    width = grad_in.shape[2]
    rounds = saved_inputs.shape[0]
    capacity = 9 * rows_dev * expert_ids.shape[-1] // (8 * groups)
    lanes = 128
    pieces = width // lanes
    columns = groups * capacity
    hidden = w_gate.shape[-1]
    gate_proj = w_gate[0, 0].reshape(pieces, lanes, hidden)
    up_proj = w_up[0, 0].reshape(pieces, lanes, hidden)
    down_proj = w_down[0, 0].reshape(hidden, pieces, lanes)
    column_ids = jnp.arange(columns, dtype=jnp.int32)

    def route_plan(step):
        route_ids = expert_ids[step, 0]
        slot_ids = slots[step, 0]
        target = jnp.where(slot_ids < capacity, route_ids * capacity + slot_ids, -1)
        hit = target[:, :, None] == column_ids[None, None, :]
        dispatch = jnp.any(hit, axis=1).T.astype(jnp.bfloat16).reshape(groups, capacity, rows_dev)
        weights = jnp.sum(jnp.where(hit, gates[step, 0][:, :, None], 0.0), axis=1)
        weights_hi = weights.astype(jnp.bfloat16)
        weights_lo = (weights - weights_hi.astype(jnp.float32)).astype(jnp.bfloat16)
        shape = (rows_dev, groups, capacity)
        return dispatch, weights_hi.reshape(shape), weights_lo.reshape(shape)

    def collect(dispatch, rows):
        picked = jnp.einsum("ect,tjl->ecjl", dispatch, rows, preferred_element_type=jnp.float32)
        return picked.astype(jnp.bfloat16)

    def exchange(buffer):
        count = buffer.shape[1]
        flat = buffer.reshape(groups, count * pieces, lanes)
        moved = lax.all_to_all(flat, "expert", split_axis=0, concat_axis=0, tiled=True)
        return moved.reshape(groups, count, pieces, lanes)

    plans = [route_plan(step) for step in range(rounds)]
    first_part = exchange(collect(plans[0][0], saved_inputs[0, 0].reshape(rows_dev, pieces, lanes)))
    bounds = [(0, capacity // 2), (capacity // 2, capacity)]
    present_block = grad_in[0].reshape(rows_dev, pieces, lanes)
    first_grads = [collect(plans[0][0][:, lo:hi], present_block) for lo, hi in bounds]
    first_part, first_grads, later_inputs = lax.optimization_barrier((first_part, first_grads, saved_inputs[1:]))
    input_buffers = [None] + [
        collect(plans[step][0], later_inputs[step - 1, 0].reshape(rows_dev, pieces, lanes))
        for step in range(1, rounds)
    ]
    pre_gate, pre_up = forward_part(first_part, gate_proj, up_proj)

    for step in range(rounds):
        dispatch, weights_hi, weights_lo = plans[step]
        if step > 0:
            next_part, present_block = lax.optimization_barrier((next_part, present_block))
        if step == 0:
            grad_parts = [exchange(buffer) for buffer in first_grads]
        else:
            grad_parts = [exchange(collect(dispatch[:, lo:hi], present_block)) for lo, hi in bounds]
        if step > 0:
            pre_gate, pre_up = forward_part(next_part, gate_proj, up_proj)
        results = [
            backward_part(grad_parts[i], pre_gate[:, lo:hi], pre_up[:, lo:hi], gate_proj, up_proj, down_proj)
            for i, (lo, hi) in enumerate(bounds)
        ]
        summed = present_block.astype(jnp.float32)
        for i, (lo, hi) in enumerate(bounds):
            arrived = exchange(results[i])
            if i + 1 == len(bounds) and step + 1 < rounds:
                arrived, next_buffer = lax.optimization_barrier((arrived, input_buffers[step + 1]))
                next_part = exchange(next_buffer)
            summed = summed + jnp.einsum(
                "tec,ecjl->tjl", weights_hi[:, :, lo:hi], arrived, preferred_element_type=jnp.float32
            )
            summed = summed + jnp.einsum(
                "tec,ecjl->tjl", weights_lo[:, :, lo:hi], arrived, preferred_element_type=jnp.float32
            )
        present_block = shifted(summed.astype(jnp.bfloat16), "section", -1)
    return present_block.reshape(1, rows_dev, width)


def solution(mesh):
    placed = (
        P("section", "expert", None),
        P(None, "section", "expert", None),
        P(None, "section", "expert", None),
        P(None, "section", "expert", None),
        P(None, "section", "expert", None),
        P("section", "expert", None, None),
        P("section", "expert", None, None),
        P("section", "expert", None, None),
    )
    return jax.shard_map(
        per_device,
        mesh=mesh,
        in_specs=placed,
        out_specs=P("section", "expert", None),
        check_vma=False,
    )
```

```python
import jax
import jax.numpy as jnp
from jax import lax
from jax.sharding import PartitionSpec as P


def shifted(x, axis, by):
    devices = lax.axis_size(axis)
    return lax.ppermute(x, axis, [(i, (i + by) % devices) for i in range(devices)])


def forward_part(input_part, gate_proj, up_proj):
    pre_gate = jnp.einsum("scjl,jlh->sch", input_part, gate_proj, preferred_element_type=jnp.float32)
    pre_up = jnp.einsum("scjl,jlh->sch", input_part, up_proj, preferred_element_type=jnp.float32)
    return pre_gate, pre_up


def backward_part(grad_part, pre_gate, pre_up, gate_proj, up_proj, down_proj):
    grad_hidden = jnp.einsum("scjl,hjl->sch", grad_part, down_proj, preferred_element_type=jnp.float32)
    sigma = jax.nn.sigmoid(pre_gate)
    derivative = sigma * (1.0 + pre_gate * (1.0 - sigma))
    grad_gate = (grad_hidden * pre_up * derivative).astype(jnp.bfloat16)
    grad_up = (grad_hidden * pre_gate * sigma).astype(jnp.bfloat16)
    summed = jnp.einsum("sch,jlh->scjl", grad_gate, gate_proj, preferred_element_type=jnp.float32)
    summed = summed + jnp.einsum("sch,jlh->scjl", grad_up, up_proj, preferred_element_type=jnp.float32)
    return summed.astype(jnp.bfloat16)


def per_device(grad_in, saved_inputs, expert_ids, slots, gates, w_gate, w_up, w_down):
    groups = lax.axis_size("expert")
    rows_dev = grad_in.shape[1]
    width = grad_in.shape[2]
    rounds = saved_inputs.shape[0]
    capacity = 9 * rows_dev * expert_ids.shape[-1] // (8 * groups)
    lanes = 128
    pieces = width // lanes
    columns = groups * capacity
    hidden = w_gate.shape[-1]
    gate_proj = w_gate[0, 0].reshape(pieces, lanes, hidden)
    up_proj = w_up[0, 0].reshape(pieces, lanes, hidden)
    down_proj = w_down[0, 0].reshape(hidden, pieces, lanes)
    column_ids = jnp.arange(columns, dtype=jnp.int32)

    def route_plan(step):
        route_ids = expert_ids[step, 0]
        slot_ids = slots[step, 0]
        target = jnp.where(slot_ids < capacity, route_ids * capacity + slot_ids, -1)
        hit = target[:, :, None] == column_ids[None, None, :]
        dispatch = jnp.any(hit, axis=1).T.astype(jnp.bfloat16).reshape(groups, capacity, rows_dev)
        weights = jnp.sum(jnp.where(hit, gates[step, 0][:, :, None], 0.0), axis=1)
        weights_hi = weights.astype(jnp.bfloat16)
        weights_lo = (weights - weights_hi.astype(jnp.float32)).astype(jnp.bfloat16)
        shape = (rows_dev, groups, capacity)
        return dispatch, weights_hi.reshape(shape), weights_lo.reshape(shape)

    def collect(dispatch, rows):
        picked = jnp.einsum("ect,tjl->ecjl", dispatch, rows, preferred_element_type=jnp.float32)
        return picked.astype(jnp.bfloat16)

    def exchange(buffer):
        count = buffer.shape[1]
        flat = buffer.reshape(groups, count * pieces, lanes)
        moved = lax.all_to_all(flat, "expert", split_axis=0, concat_axis=0, tiled=True)
        return moved.reshape(groups, count, pieces, lanes)

    plans = [route_plan(step) for step in range(rounds)]
    first_part = exchange(collect(plans[0][0], saved_inputs[0, 0].reshape(rows_dev, pieces, lanes)))
    first_part, first_block, later_inputs, down_raw = lax.optimization_barrier(
        (first_part, grad_in[0], saved_inputs[1:], w_down[0, 0])
    )
    down_proj = down_raw.reshape(hidden, pieces, lanes)
    input_buffers = [None] + [
        collect(plans[step][0], later_inputs[step - 1, 0].reshape(rows_dev, pieces, lanes))
        for step in range(1, rounds)
    ]
    pre_gate, pre_up = forward_part(first_part, gate_proj, up_proj)
    bounds = [(0, capacity // 2), (capacity // 2, capacity)]

    present_block = first_block.reshape(rows_dev, pieces, lanes)
    for step in range(rounds):
        dispatch, weights_hi, weights_lo = plans[step]
        if step > 0:
            next_part, present_block = lax.optimization_barrier((next_part, present_block))
        grad_parts = [exchange(collect(dispatch[:, lo:hi], present_block)) for lo, hi in bounds]
        if step > 0:
            pre_gate, pre_up = forward_part(next_part, gate_proj, up_proj)
        results = [
            backward_part(grad_parts[i], pre_gate[:, lo:hi], pre_up[:, lo:hi], gate_proj, up_proj, down_proj)
            for i, (lo, hi) in enumerate(bounds)
        ]
        summed = present_block.astype(jnp.float32)
        for i, (lo, hi) in enumerate(bounds):
            arrived = exchange(results[i])
            if i + 1 == len(bounds) and step + 1 < rounds:
                arrived, next_buffer = lax.optimization_barrier((arrived, input_buffers[step + 1]))
                next_part = exchange(next_buffer)
            summed = summed + jnp.einsum(
                "tec,ecjl->tjl", weights_hi[:, :, lo:hi], arrived, preferred_element_type=jnp.float32
            )
            summed = summed + jnp.einsum(
                "tec,ecjl->tjl", weights_lo[:, :, lo:hi], arrived, preferred_element_type=jnp.float32
            )
        present_block = shifted(summed.astype(jnp.bfloat16), "section", -1)
    return present_block.reshape(1, rows_dev, width)


def solution(mesh):
    placed = (
        P("section", "expert", None),
        P(None, "section", "expert", None),
        P(None, "section", "expert", None),
        P(None, "section", "expert", None),
        P(None, "section", "expert", None),
        P("section", "expert", None, None),
        P("section", "expert", None, None),
        P("section", "expert", None, None),
    )
    return jax.shard_map(
        per_device,
        mesh=mesh,
        in_specs=placed,
        out_specs=P("section", "expert", None),
        check_vma=False,
    )
```

```python
import jax
import jax.numpy as jnp
from jax import lax
from jax.sharding import PartitionSpec as P


def shifted(x, axis, by):
    devices = lax.axis_size(axis)
    return lax.ppermute(x, axis, [(i, (i + by) % devices) for i in range(devices)])


def forward_part(input_part, gate_proj, up_proj):
    pre_gate = jnp.einsum("scjl,jlh->sch", input_part, gate_proj, preferred_element_type=jnp.float32)
    pre_up = jnp.einsum("scjl,jlh->sch", input_part, up_proj, preferred_element_type=jnp.float32)
    return pre_gate, pre_up


def backward_part(grad_part, pre_gate, pre_up, gate_proj, up_proj, down_proj):
    grad_hidden = jnp.einsum("scjl,hjl->sch", grad_part, down_proj, preferred_element_type=jnp.float32)
    sigma = jax.nn.sigmoid(pre_gate)
    derivative = sigma * (1.0 + pre_gate * (1.0 - sigma))
    grad_gate = (grad_hidden * pre_up * derivative).astype(jnp.bfloat16)
    grad_up = (grad_hidden * pre_gate * sigma).astype(jnp.bfloat16)
    summed = jnp.einsum("sch,jlh->scjl", grad_gate, gate_proj, preferred_element_type=jnp.float32)
    summed = summed + jnp.einsum("sch,jlh->scjl", grad_up, up_proj, preferred_element_type=jnp.float32)
    return summed.astype(jnp.bfloat16)


def per_device(grad_in, saved_inputs, expert_ids, slots, gates, w_gate, w_up, w_down):
    groups = lax.axis_size("expert")
    rows_dev = grad_in.shape[1]
    width = grad_in.shape[2]
    rounds = saved_inputs.shape[0]
    capacity = 9 * rows_dev * expert_ids.shape[-1] // (8 * groups)
    lanes = 128
    pieces = width // lanes
    columns = groups * capacity
    hidden = w_gate.shape[-1]
    gate_proj = w_gate[0, 0].reshape(pieces, lanes, hidden)
    up_proj = w_up[0, 0].reshape(pieces, lanes, hidden)
    down_proj = w_down[0, 0].reshape(hidden, pieces, lanes)
    column_ids = jnp.arange(columns, dtype=jnp.int32)

    def route_plan(step):
        route_ids = expert_ids[step, 0]
        slot_ids = slots[step, 0]
        target = jnp.where(slot_ids < capacity, route_ids * capacity + slot_ids, -1)
        hit = target[:, :, None] == column_ids[None, None, :]
        dispatch = jnp.any(hit, axis=1).T.astype(jnp.bfloat16).reshape(groups, capacity, rows_dev)
        weights = jnp.sum(jnp.where(hit, gates[step, 0][:, :, None], 0.0), axis=1)
        weights_hi = weights.astype(jnp.bfloat16)
        weights_lo = (weights - weights_hi.astype(jnp.float32)).astype(jnp.bfloat16)
        shape = (rows_dev, groups, capacity)
        return dispatch, weights_hi.reshape(shape), weights_lo.reshape(shape)

    def collect(dispatch, rows):
        picked = jnp.einsum("ect,tjl->ecjl", dispatch, rows, preferred_element_type=jnp.float32)
        return picked.astype(jnp.bfloat16)

    def exchange(buffer):
        count = buffer.shape[1]
        flat = buffer.reshape(groups, count * pieces, lanes)
        moved = lax.all_to_all(flat, "expert", split_axis=0, concat_axis=0, tiled=True)
        return moved.reshape(groups, count, pieces, lanes)

    plans = [route_plan(step) for step in range(rounds)]
    first_part = exchange(collect(plans[0][0], saved_inputs[0, 0].reshape(rows_dev, pieces, lanes)))
    first_part, first_block, later_inputs, down_raw, gate_raw, up_raw = lax.optimization_barrier(
        (first_part, grad_in[0], saved_inputs[1:], w_down[0, 0], w_gate[0, 0], w_up[0, 0])
    )
    down_proj = down_raw.reshape(hidden, pieces, lanes)
    gate_proj = gate_raw.reshape(pieces, lanes, hidden)
    up_proj = up_raw.reshape(pieces, lanes, hidden)
    input_buffers = [None] + [
        collect(plans[step][0], later_inputs[step - 1, 0].reshape(rows_dev, pieces, lanes))
        for step in range(1, rounds)
    ]
    pre_gate, pre_up = forward_part(first_part, gate_proj, up_proj)
    bounds = [(0, capacity // 2), (capacity // 2, capacity)]

    present_block = first_block.reshape(rows_dev, pieces, lanes)
    for step in range(rounds):
        dispatch, weights_hi, weights_lo = plans[step]
        if step > 0:
            next_part, present_block = lax.optimization_barrier((next_part, present_block))
        grad_parts = [exchange(collect(dispatch[:, lo:hi], present_block)) for lo, hi in bounds]
        if step > 0:
            pre_gate, pre_up = forward_part(next_part, gate_proj, up_proj)
        results = [
            backward_part(grad_parts[i], pre_gate[:, lo:hi], pre_up[:, lo:hi], gate_proj, up_proj, down_proj)
            for i, (lo, hi) in enumerate(bounds)
        ]
        summed = present_block.astype(jnp.float32)
        for i, (lo, hi) in enumerate(bounds):
            arrived = exchange(results[i])
            if i + 1 == len(bounds) and step + 1 < rounds:
                arrived, next_buffer = lax.optimization_barrier((arrived, input_buffers[step + 1]))
                next_part = exchange(next_buffer)
            summed = summed + jnp.einsum(
                "tec,ecjl->tjl", weights_hi[:, :, lo:hi], arrived, preferred_element_type=jnp.float32
            )
            summed = summed + jnp.einsum(
                "tec,ecjl->tjl", weights_lo[:, :, lo:hi], arrived, preferred_element_type=jnp.float32
            )
        present_block = shifted(summed.astype(jnp.bfloat16), "section", -1)
    return present_block.reshape(1, rows_dev, width)


def solution(mesh):
    placed = (
        P("section", "expert", None),
        P(None, "section", "expert", None),
        P(None, "section", "expert", None),
        P(None, "section", "expert", None),
        P(None, "section", "expert", None),
        P("section", "expert", None, None),
        P("section", "expert", None, None),
        P("section", "expert", None, None),
    )
    return jax.shard_map(
        per_device,
        mesh=mesh,
        in_specs=placed,
        out_specs=P("section", "expert", None),
        check_vma=False,
    )
```
